128 devices in a mesh: rcv: 16 (over y_hi, x, core), win: 8 (over z, y_lo).
Axes of the slice: x: 4, y: 4 (y_hi: 2, y_lo: 2; y = y_hi * 2 + y_lo), z: 4, core: 2. Of those that a mesh axis runs over, the one named last changes fastest.
Arguments:
- traces: bfloat16 [8192, 8, 6144], P('rcv', 'win'), may hold values from -6 to 6
- sources: int32 [8, 4], replicated, may hold values from 0 to 8191
- offsets: int32 [8], P('win'), may hold values from 0 to 44
Outputs:
- stacks: float32 [32, 101, 8192], P('win', None, 'rcv')
The draws below stay inside these ranges and needn't reach their ends.
All inputs are finite; a program needn't handle non-finite values.
Results may differ from the reference program's by a relative error of at most 0.0003.
Values may be sent and summed in bfloat16 or wider, within the bound.
No kernel may reach another device: no remote copies, remote signals or barrier semaphores. Data moves between devices by JAX's collectives and lax.ppermute only.
A program may use at most 192 MiB of HBM per device.

```python
import math
import jax
import jax.numpy as jnp
from jax import lax

SAMPLES = 6000
HALF = 50
PAD = 44
STEPS = 8
SRC = 4
LAGS = 101
SPAN = 6144
CHANNELS = 8192
WINDOWS = 8


def touch_ends(array, stream_key, least, high):
    longest = array.shape.index(max(array.shape))
    spots = []
    for shift in (0, 1):
        where = [jax.random.randint(jax.random.fold_in(stream_key, axis), (), 0, length) for axis, length in enumerate(array.shape)]
        where[longest] = (where[longest] + shift) % array.shape[longest]
        spots.append(tuple(where))
    return array.at[spots[0]].set(least).at[spots[1]].set(high)


def shard_levels(stream_key, extent, cuts, least, largest):
    level = 1.0
    for position, shards_of in cuts:
        steps = jax.random.uniform(jax.random.fold_in(jax.random.fold_in(stream_key, 6), position), (shards_of,), jnp.float32, least / len(cuts), largest / len(cuts))
        level = level * jnp.repeat(jnp.exp(steps), extent[position] // shards_of).reshape((-1,) + (1,) * (len(extent) - 1 - position))
    return level


def scatter_about(rng, shape, scale, limit, split=(), kind=jnp.bfloat16):
    values = jax.random.normal(rng, shape, jnp.float32) * scale
    if len(split) > 0:
        values = shard_levels(rng, shape, split, -0.22, 0.18) * values
    return jnp.clip(values, min=-limit, max=limit).astype(kind)


def setup_inputs(seed: int = 0) -> dict:
    key_of = jax.random.split(jax.random.key(seed), 4)
    traces = scatter_about(key_of[0], (CHANNELS, WINDOWS, SPAN), 1.0, 6.0, ((0, 16), (1, 8)))
    sources = touch_ends(jax.random.randint(key_of[1], (STEPS, SRC), 0, CHANNELS), jax.random.fold_in(key_of[1], 1), 0, CHANNELS - 1).astype(jnp.int32)
    offsets = touch_ends(jax.random.randint(key_of[2], (WINDOWS,), 0, PAD + 1), jax.random.fold_in(key_of[2], 1), 0, PAD).astype(jnp.int32)
    return {"traces": traces, "sources": sources, "offsets": offsets}


def lagged(signal):
    leading = signal.shape[:-1]
    padded = jnp.concatenate([signal, jnp.zeros(leading + (2 * HALF + 1,), signal.dtype)], axis=-1)
    span_len = padded.shape[-1]
    tiled = jnp.tile(padded, (1,) * len(leading) + (LAGS,))
    return tiled[..., :LAGS * (span_len - 1)].reshape(leading + (LAGS, span_len - 1))

def reference(traces, sources, offsets):
    source_all = traces[sources.reshape(-1).astype(jnp.int32)]

    def one_window(summed, window):
        start_at = offsets[window].astype(jnp.int32)
        source_win = lax.dynamic_index_in_dim(source_all, window, 1, keepdims=False)
        trace_win = lax.dynamic_index_in_dim(traces, window, 1, keepdims=False)
        source_cut = lax.dynamic_slice_in_dim(source_win, start_at + HALF, SAMPLES, 1)
        receiver = lax.dynamic_slice_in_dim(trace_win, start_at, SAMPLES + 2 * HALF, 1)
        term = jnp.einsum('kjt,ct->kjc', lagged(source_cut).astype(jnp.float32), receiver.astype(jnp.float32))
        return (summed + term, None)
    initial = jnp.zeros((STEPS * SRC, LAGS, CHANNELS), jnp.float32)
    summed, _ = lax.scan(one_window, initial, jnp.arange(WINDOWS, dtype=jnp.int32))
    return summed * (1.0 / math.sqrt(SAMPLES * WINDOWS))
```

```python
import math

import jax
import jax.numpy as jnp
from jax import lax
from jax.experimental import pallas as pl
from jax.experimental.pallas import tpu as pltpu
from jax.sharding import PartitionSpec as P

SAMPLES = 6000
HALF = 50
LAGS = 101
ROWS = 128
LANE = 128
FRONT = ROWS - HALF
CHUNK = 1024


def corr_kernel(mq_ref, rt_ref, out_ref, acc_ref, *, scale, pairs, width):
    q = pl.program_id(0)
    u0 = pl.multiple_of(q * width, LANE)
    row = lax.broadcasted_iota(jnp.int32, (ROWS, LANE), 0)
    lane = lax.broadcasted_iota(jnp.int32, (ROWS, LANE), 1)
    keep = lane >= row
    blocks = width // LANE

    def lagged(k):
        line = mq_ref[pl.ds(k, 1), pl.ds(u0, width + LANE)]
        wide = jnp.broadcast_to(line, (ROWS, width + LANE))
        turned = [
            pltpu.roll(wide[:, b * LANE : (b + 1) * LANE], 0, 1, stride=1, stride_axis=0)
            for b in range(blocks + 1)
        ]
        parts = [jnp.where(keep, turned[b + 1], turned[b]) for b in range(blocks)]
        return jnp.concatenate(parts, axis=1).astype(jnp.bfloat16)

    def body(p, carry):
        lhs = jnp.concatenate([lagged(2 * p), lagged(2 * p + 1)], axis=0)
        prod = jnp.dot(lhs, rt_ref[...], preferred_element_type=jnp.float32)

        @pl.when(q == 0)
        def _():
            acc_ref[p] = prod

        @pl.when(q > 0)
        def _():
            acc_ref[p] = acc_ref[p] + prod

        return carry

    lax.fori_loop(0, pairs, body, 0)

    @pl.when(q == pl.num_programs(0) - 1)
    def _():
        for k in range(2 * pairs):
            half = (k % 2) * ROWS
            out_ref[k] = acc_ref[k // 2, half : half + LAGS, :] * scale


def correlate(mq, rt, scale):
    n_src = mq.shape[0]
    span, ch = rt.shape
    pairs = n_src // 2
    width = CHUNK if span % CHUNK == 0 else span
    kernel = lambda *refs: corr_kernel(*refs, scale=scale, pairs=pairs, width=width)
    return pl.pallas_call(
        kernel,
        grid=(span // width,),
        in_specs=[
            pl.BlockSpec(mq.shape, lambda q: (0, 0)),
            pl.BlockSpec((width, ch), lambda q: (q, 0)),
        ],
        out_specs=pl.BlockSpec((n_src, LAGS, ch), lambda q: (0, 0, 0)),
        out_shape=jax.ShapeDtypeStruct((n_src, LAGS, ch), jnp.float32),
        scratch_shapes=[pltpu.VMEM((pairs, 2 * ROWS, ch), jnp.float32)],
        compiler_params=pltpu.CompilerParams(dimension_semantics=("arbitrary",)),
    )(mq, rt)


def shards(traces, sources, offsets):
    ch_dev = traces.shape[0]
    span = traces.shape[2]
    win_count = lax.axis_size("win")
    first_row = lax.axis_index("rcv") * ch_dev
    norm_scale = 1.0 / math.sqrt(SAMPLES * traces.shape[1] * win_count)
    record = traces[:, 0, :]
    channel_ids = jnp.arange(ch_dev, dtype=jnp.int32)
    select = (sources.reshape(-1)[:, None] - first_row == channel_ids[None, :]).astype(
        traces.dtype
    )
    picked = jnp.dot(select, record, preferred_element_type=jnp.float32).astype(jnp.bfloat16)
    source_rows = lax.psum(picked, "rcv")
    start_at = offsets[0]
    positions = jnp.arange(span, dtype=jnp.int32)
    inside = (positions >= start_at + HALF) & (positions < start_at + HALF + SAMPLES)
    masked = jnp.where(inside[None, :], source_rows, jnp.zeros_like(source_rows))
    mq = jnp.pad(masked.astype(jnp.float32), ((0, 0), (FRONT, LANE - FRONT)))
    stacked = correlate(mq, record.T, norm_scale)
    return lax.psum_scatter(stacked, "win", scatter_dimension=0, tiled=True)


def solution(mesh):
    in_specs = (P("rcv", "win", None), P(), P("win"))
    out_specs = P("win", None, "rcv")
    return jax.shard_map(shards, mesh=mesh, in_specs=in_specs, out_specs=out_specs, check_vma=False)
```

```python
import math

import jax
import jax.numpy as jnp
from jax import lax
from jax.experimental import pallas as pl
from jax.experimental.pallas import tpu as pltpu
from jax.sharding import PartitionSpec as P

SAMPLES = 6000
HALF = 50
LAGS = 101
ROWS = 128
LANE = 128
FRONT = ROWS - HALF
CHUNK = 1024


def corr_kernel(mq_ref, rt_ref, out_ref, acc_ref, *, scale, pairs, width):
    q = pl.program_id(0)
    u0 = pl.multiple_of(q * width, LANE)
    row = lax.broadcasted_iota(jnp.int32, (ROWS, LANE), 0)
    lane = lax.broadcasted_iota(jnp.int32, (ROWS, LANE), 1)
    keep = lane >= row
    blocks = width // LANE

    def lagged(k):
        line = mq_ref[pl.ds(k, 1), pl.ds(u0, width + LANE)]
        wide = jnp.broadcast_to(line, (ROWS, width + LANE))
        turned = [
            pltpu.roll(wide[:, b * LANE : (b + 1) * LANE], 0, 1, stride=1, stride_axis=0)
            for b in range(blocks + 1)
        ]
        parts = [jnp.where(keep, turned[b + 1], turned[b]) for b in range(blocks)]
        return jnp.concatenate(parts, axis=1).astype(jnp.bfloat16)

    def body(p, carry):
        lhs = jnp.concatenate([lagged(2 * p), lagged(2 * p + 1)], axis=0)
        prod = jnp.dot(lhs, rt_ref[...], preferred_element_type=jnp.float32)

        @pl.when(q == 0)
        def _():
            acc_ref[p] = prod

        @pl.when(q > 0)
        def _():
            acc_ref[p] = acc_ref[p] + prod

        return carry

    lax.fori_loop(0, pairs, body, 0)

    @pl.when(q == pl.num_programs(0) - 1)
    def _():
        for k in range(2 * pairs):
            half = (k % 2) * ROWS
            out_ref[k] = acc_ref[k // 2, half : half + LAGS, :] * scale


def correlate(mq, rt, scale):
    n_src = mq.shape[0]
    span, ch = rt.shape
    pairs = n_src // 2
    width = CHUNK if span % CHUNK == 0 else span
    kernel = lambda *refs: corr_kernel(*refs, scale=scale, pairs=pairs, width=width)
    return pl.pallas_call(
        kernel,
        grid=(span // width,),
        in_specs=[
            pl.BlockSpec(mq.shape, lambda q: (0, 0)),
            pl.BlockSpec((width, ch), lambda q: (q, 0)),
        ],
        out_specs=pl.BlockSpec((n_src, LAGS, ch), lambda q: (0, 0, 0)),
        out_shape=jax.ShapeDtypeStruct((n_src, LAGS, ch), jnp.float32),
        scratch_shapes=[pltpu.VMEM((pairs, 2 * ROWS, ch), jnp.float32)],
        compiler_params=pltpu.CompilerParams(dimension_semantics=("arbitrary",)),
    )(mq, rt)


def gather_sources(picked):
    parts = lax.axis_size("rcv")
    rows, span = picked.shape
    pieces = picked.reshape(rows, parts, span // parts).transpose(1, 0, 2)
    own = lax.all_to_all(pieces, "rcv", 0, 0).sum(axis=0, dtype=jnp.float32)
    spread = jnp.broadcast_to(own.astype(picked.dtype)[None], (parts,) + own.shape)
    every = lax.all_to_all(spread, "rcv", 0, 0)
    return every.transpose(1, 0, 2).reshape(rows, span)


def shards(traces, sources, offsets):
    ch_dev = traces.shape[0]
    span = traces.shape[2]
    win_count = lax.axis_size("win")
    first_row = lax.axis_index("rcv") * ch_dev
    norm_scale = 1.0 / math.sqrt(SAMPLES * traces.shape[1] * win_count)
    record = traces[:, 0, :]
    channel_ids = jnp.arange(ch_dev, dtype=jnp.int32)
    select = (sources.reshape(-1)[:, None] - first_row == channel_ids[None, :]).astype(
        traces.dtype
    )
    picked = jnp.dot(select, record, preferred_element_type=jnp.float32).astype(jnp.bfloat16)
    source_rows = gather_sources(picked)
    start_at = offsets[0]
    positions = jnp.arange(span, dtype=jnp.int32)
    inside = (positions >= start_at + HALF) & (positions < start_at + HALF + SAMPLES)
    masked = jnp.where(inside[None, :], source_rows, jnp.zeros_like(source_rows))
    mq = jnp.pad(masked.astype(jnp.float32), ((0, 0), (FRONT, LANE - FRONT)))
    stacked = correlate(mq, record.T, norm_scale)
    groups = stacked.reshape((win_count, -1) + stacked.shape[1:])
    return lax.all_to_all(groups, "win", 0, 0).sum(axis=0)


def solution(mesh):
    in_specs = (P("rcv", "win", None), P(), P("win"))
    out_specs = P("win", None, "rcv")
    return jax.shard_map(shards, mesh=mesh, in_specs=in_specs, out_specs=out_specs, check_vma=False)
```

```python
import math

import jax
import jax.numpy as jnp
from jax import lax
from jax.experimental import pallas as pl
from jax.experimental.pallas import tpu as pltpu
from jax.sharding import PartitionSpec as P

SAMPLES = 6000
HALF = 50
LAGS = 101
ROWS = 128
LANE = 128
FRONT = ROWS - HALF
CHUNK = 1024


def corr_kernel(mq_ref, rt_ref, out_ref, acc_ref, *, scale, pairs, width):
    q = pl.program_id(0)
    u0 = pl.multiple_of(q * width, LANE)
    row = lax.broadcasted_iota(jnp.int32, (ROWS, LANE), 0)
    lane = lax.broadcasted_iota(jnp.int32, (ROWS, LANE), 1)
    keep = lane >= row
    blocks = width // LANE

    def lagged(k):
        line = mq_ref[pl.ds(k, 1), pl.ds(u0, width + LANE)]
        wide = jnp.broadcast_to(line, (ROWS, width + LANE))
        turned = [
            pltpu.roll(wide[:, b * LANE : (b + 1) * LANE], 0, 1, stride=1, stride_axis=0)
            for b in range(blocks + 1)
        ]
        parts = [jnp.where(keep, turned[b + 1], turned[b]) for b in range(blocks)]
        return jnp.concatenate(parts, axis=1).astype(jnp.bfloat16)

    def body(p, carry):
        lhs = jnp.concatenate([lagged(2 * p), lagged(2 * p + 1)], axis=0)
        prod = lax.dot_general(
            lhs, rt_ref[...], (((1,), (1,)), ((), ())), preferred_element_type=jnp.float32
        )

        @pl.when(q == 0)
        def _():
            acc_ref[p] = prod

        @pl.when(q > 0)
        def _():
            acc_ref[p] = acc_ref[p] + prod

        return carry

    lax.fori_loop(0, pairs, body, 0)

    @pl.when(q == pl.num_programs(0) - 1)
    def _():
        for k in range(2 * pairs):
            half = (k % 2) * ROWS
            out_ref[k] = acc_ref[k // 2, half : half + LAGS, :] * scale


def correlate(mq, traces, scale):
    n_src = mq.shape[0]
    ch, _, span = traces.shape
    pairs = n_src // 2
    width = CHUNK if span % CHUNK == 0 else span
    kernel = lambda *refs: corr_kernel(*refs, scale=scale, pairs=pairs, width=width)
    return pl.pallas_call(
        kernel,
        grid=(span // width,),
        in_specs=[
            pl.BlockSpec(mq.shape, lambda q: (0, 0)),
            pl.BlockSpec((ch, None, width), lambda q: (0, 0, q)),
        ],
        out_specs=pl.BlockSpec((n_src, LAGS, ch), lambda q: (0, 0, 0)),
        out_shape=jax.ShapeDtypeStruct((n_src, LAGS, ch), jnp.float32),
        scratch_shapes=[pltpu.VMEM((pairs, 2 * ROWS, ch), jnp.float32)],
        compiler_params=pltpu.CompilerParams(dimension_semantics=("arbitrary",)),
    )(mq, traces)


def gather_sources(picked):
    parts = lax.axis_size("rcv")
    rows, span = picked.shape
    pieces = picked.reshape(rows, parts, span // parts).transpose(1, 0, 2)
    own = lax.all_to_all(pieces, "rcv", 0, 0).sum(axis=0, dtype=jnp.float32)
    spread = jnp.broadcast_to(own.astype(picked.dtype)[None], (parts,) + own.shape)
    every = lax.all_to_all(spread, "rcv", 0, 0)
    return every.transpose(1, 0, 2).reshape(rows, span)


def shards(traces, sources, offsets):
    ch_dev = traces.shape[0]
    span = traces.shape[2]
    win_count = lax.axis_size("win")
    first_row = lax.axis_index("rcv") * ch_dev
    norm_scale = 1.0 / math.sqrt(SAMPLES * traces.shape[1] * win_count)
    record = traces[:, 0, :]
    channel_ids = jnp.arange(ch_dev, dtype=jnp.int32)
    select = (sources.reshape(-1)[:, None] - first_row == channel_ids[None, :]).astype(
        traces.dtype
    )
    picked = jnp.dot(select, record, preferred_element_type=jnp.float32).astype(jnp.bfloat16)
    source_rows = gather_sources(picked)
    start_at = offsets[0]
    positions = jnp.arange(span, dtype=jnp.int32)
    inside = (positions >= start_at + HALF) & (positions < start_at + HALF + SAMPLES)
    masked = jnp.where(inside[None, :], source_rows, jnp.zeros_like(source_rows))
    mq = jnp.pad(masked.astype(jnp.float32), ((0, 0), (FRONT, LANE - FRONT)))
    per_group = mq.shape[0] // win_count
    by_group = mq.reshape(win_count, per_group, mq.shape[1])
    outs = []
    for i in range(per_group):
        part = correlate(by_group[:, i, :], traces, norm_scale)
        outs.append(lax.all_to_all(part, "win", 0, 0).sum(axis=0))
    return jnp.stack(outs, axis=0)


def solution(mesh):
    in_specs = (P("rcv", "win", None), P(), P("win"))
    out_specs = P("win", None, "rcv")
    return jax.shard_map(shards, mesh=mesh, in_specs=in_specs, out_specs=out_specs, check_vma=False)
```

```python
import math

import jax
import jax.numpy as jnp
from jax import lax
from jax.experimental import pallas as pl
from jax.experimental.pallas import tpu as pltpu
from jax.sharding import PartitionSpec as P

SAMPLES = 6000
HALF = 50
LAGS = 101
ROWS = 128
LANE = 128
FRONT = ROWS - HALF
CHUNK = 1024


def corr_kernel(mq_ref, rt_ref, out_ref, acc_ref, *, scale, pairs, width):
    q = pl.program_id(0)
    u0 = pl.multiple_of(q * width, LANE)
    row = lax.broadcasted_iota(jnp.int32, (ROWS, LANE), 0)
    lane = lax.broadcasted_iota(jnp.int32, (ROWS, LANE), 1)
    keep = lane >= row
    blocks = width // LANE

    def lagged(k):
        line = mq_ref[pl.ds(k, 1), pl.ds(u0, width + LANE)]
        wide = jnp.broadcast_to(line, (ROWS, width + LANE))
        turned = [
            pltpu.roll(wide[:, b * LANE : (b + 1) * LANE], 0, 1, stride=1, stride_axis=0)
            for b in range(blocks + 1)
        ]
        parts = [jnp.where(keep, turned[b + 1], turned[b]) for b in range(blocks)]
        return jnp.concatenate(parts, axis=1).astype(jnp.bfloat16)

    def body(p, carry):
        lhs = jnp.concatenate([lagged(2 * p), lagged(2 * p + 1)], axis=0)
        prod = jnp.dot(lhs, rt_ref[...], preferred_element_type=jnp.float32)

        @pl.when(q == 0)
        def _():
            acc_ref[p] = prod

        @pl.when(q > 0)
        def _():
            acc_ref[p] = acc_ref[p] + prod

        return carry

    lax.fori_loop(0, pairs, body, 0)

    @pl.when(q == pl.num_programs(0) - 1)
    def _():
        for k in range(2 * pairs):
            half = (k % 2) * ROWS
            out_ref[k] = acc_ref[k // 2, half : half + LAGS, :] * scale


def correlate(mq, rt, scale):
    n_src = mq.shape[0]
    span, ch = rt.shape
    pairs = n_src // 2
    width = CHUNK if span % CHUNK == 0 else span
    kernel = lambda *refs: corr_kernel(*refs, scale=scale, pairs=pairs, width=width)
    return pl.pallas_call(
        kernel,
        grid=(span // width,),
        in_specs=[
            pl.BlockSpec(mq.shape, lambda q: (0, 0)),
            pl.BlockSpec((width, ch), lambda q: (q, 0)),
        ],
        out_specs=pl.BlockSpec((n_src, LAGS, ch), lambda q: (0, 0, 0)),
        out_shape=jax.ShapeDtypeStruct((n_src, LAGS, ch), jnp.float32),
        scratch_shapes=[pltpu.VMEM((pairs, 2 * ROWS, ch), jnp.float32)],
        compiler_params=pltpu.CompilerParams(dimension_semantics=("arbitrary",)),
    )(mq, rt)


def gather_sources(picked):
    parts = lax.axis_size("rcv")
    rows, span = picked.shape
    pieces = picked.reshape(rows, parts, span // parts).transpose(1, 0, 2)
    own = lax.all_to_all(pieces, "rcv", 0, 0).sum(axis=0, dtype=jnp.float32)
    spread = jnp.broadcast_to(own.astype(picked.dtype)[None], (parts,) + own.shape)
    every = lax.all_to_all(spread, "rcv", 0, 0)
    return every.transpose(1, 0, 2).reshape(rows, span)


def shards(traces, sources, offsets):
    ch_dev = traces.shape[0]
    span = traces.shape[2]
    win_count = lax.axis_size("win")
    first_row = lax.axis_index("rcv") * ch_dev
    norm_scale = 1.0 / math.sqrt(SAMPLES * traces.shape[1] * win_count)
    record = traces[:, 0, :]
    channel_ids = jnp.arange(ch_dev, dtype=jnp.int32)
    select = (sources.reshape(-1)[:, None] - first_row == channel_ids[None, :]).astype(
        traces.dtype
    )
    picked = jnp.dot(select, record, preferred_element_type=jnp.float32).astype(jnp.bfloat16)
    source_rows = gather_sources(picked)
    start_at = offsets[0]
    positions = jnp.arange(span, dtype=jnp.int32)
    inside = (positions >= start_at + HALF) & (positions < start_at + HALF + SAMPLES)
    masked = jnp.where(inside[None, :], source_rows, jnp.zeros_like(source_rows))
    mq = jnp.pad(masked.astype(jnp.float32), ((0, 0), (FRONT, LANE - FRONT)))
    per_group = mq.shape[0] // win_count
    by_group = mq.reshape(win_count, per_group, mq.shape[1])
    rt = record.T
    outs = []
    for i in range(per_group):
        part = correlate(by_group[:, i, :], rt, norm_scale)
        outs.append(lax.all_to_all(part, "win", 0, 0).sum(axis=0))
    return jnp.stack(outs, axis=0)


def solution(mesh):
    in_specs = (P("rcv", "win", None), P(), P("win"))
    out_specs = P("win", None, "rcv")
    return jax.shard_map(shards, mesh=mesh, in_specs=in_specs, out_specs=out_specs, check_vma=False)
```

```python
import math

import jax
import jax.numpy as jnp
from jax import lax
from jax.experimental import pallas as pl
from jax.experimental.pallas import tpu as pltpu
from jax.sharding import PartitionSpec as P

SAMPLES = 6000
HALF = 50
LAGS = 101
ROWS = 128
LANE = 128
FRONT = ROWS - HALF
CHUNK = 2048


def corr_kernel(mq_ref, rt_ref, out_ref, acc_ref, lag_ref, *, scale, pairs, width):
    q = pl.program_id(0)
    u0 = pl.multiple_of(q * width, LANE)
    row = lax.broadcasted_iota(jnp.int32, (ROWS, LANE), 0)
    lane = lax.broadcasted_iota(jnp.int32, (ROWS, LANE), 1)
    keep = lane >= row
    blocks = width // LANE

    def turned(k, b):
        line = mq_ref[pl.ds(k, 1), pl.ds(u0 + b * LANE, LANE)]
        return pltpu.roll(jnp.broadcast_to(line, (ROWS, LANE)), 0, 1, stride=1, stride_axis=0)

    def build(k, slot, half):
        prev = turned(k, 0)
        for b in range(blocks):
            cur = turned(k, b + 1)
            lag_ref[slot, half * ROWS : (half + 1) * ROWS, b * LANE : (b + 1) * LANE] = jnp.where(
                keep, cur, prev
            ).astype(jnp.bfloat16)
            prev = cur

    @pl.when(q == 0)
    def _():
        acc_ref[...] = jnp.zeros_like(acc_ref)

    for p in range(pairs):
        slot = p % 2
        build(2 * p, slot, 0)
        build(2 * p + 1, slot, 1)
        acc_ref[p] += jnp.dot(lag_ref[slot], rt_ref[...], preferred_element_type=jnp.float32)

    @pl.when(q == pl.num_programs(0) - 1)
    def _():
        for k in range(2 * pairs):
            half = (k % 2) * ROWS
            out_ref[k] = acc_ref[k // 2, half : half + LAGS, :] * scale


def correlate(mq, rt, scale):
    n_src = mq.shape[0]
    span, ch = rt.shape
    pairs = n_src // 2
    width = CHUNK if span % CHUNK == 0 else span
    kernel = lambda *refs: corr_kernel(*refs, scale=scale, pairs=pairs, width=width)
    return pl.pallas_call(
        kernel,
        grid=(span // width,),
        in_specs=[
            pl.BlockSpec(mq.shape, lambda q: (0, 0)),
            pl.BlockSpec((width, ch), lambda q: (q, 0)),
        ],
        out_specs=pl.BlockSpec((n_src, LAGS, ch), lambda q: (0, 0, 0)),
        out_shape=jax.ShapeDtypeStruct((n_src, LAGS, ch), jnp.float32),
        scratch_shapes=[
            pltpu.VMEM((pairs, 2 * ROWS, ch), jnp.float32),
            pltpu.VMEM((2, 2 * ROWS, width), jnp.bfloat16),
        ],
        compiler_params=pltpu.CompilerParams(dimension_semantics=("arbitrary",)),
    )(mq, rt)


def gather_sources(picked):
    parts = lax.axis_size("rcv")
    rows, span = picked.shape
    pieces = picked.reshape(rows, parts, span // parts).transpose(1, 0, 2)
    own = lax.all_to_all(pieces, "rcv", 0, 0).sum(axis=0, dtype=jnp.float32)
    spread = jnp.broadcast_to(own.astype(picked.dtype)[None], (parts,) + own.shape)
    every = lax.all_to_all(spread, "rcv", 0, 0)
    return every.transpose(1, 0, 2).reshape(rows, span)


def shards(traces, sources, offsets):
    ch_dev = traces.shape[0]
    span = traces.shape[2]
    win_count = lax.axis_size("win")
    first_row = lax.axis_index("rcv") * ch_dev
    norm_scale = 1.0 / math.sqrt(SAMPLES * traces.shape[1] * win_count)
    record = traces[:, 0, :]
    channel_ids = jnp.arange(ch_dev, dtype=jnp.int32)
    select = (sources.reshape(-1)[:, None] - first_row == channel_ids[None, :]).astype(
        traces.dtype
    )
    picked = jnp.dot(select, record, preferred_element_type=jnp.float32).astype(jnp.bfloat16)
    source_rows = gather_sources(picked)
    start_at = offsets[0]
    positions = jnp.arange(span, dtype=jnp.int32)
    inside = (positions >= start_at + HALF) & (positions < start_at + HALF + SAMPLES)
    masked = jnp.where(inside[None, :], source_rows, jnp.zeros_like(source_rows))
    mq = jnp.pad(masked.astype(jnp.float32), ((0, 0), (FRONT, LANE - FRONT)))
    per_group = mq.shape[0] // win_count
    by_group = mq.reshape(win_count, per_group, mq.shape[1])
    rt = record.T
    outs = []
    for i in range(per_group):
        part = correlate(by_group[:, i, :], rt, norm_scale)
        outs.append(lax.all_to_all(part, "win", 0, 0).sum(axis=0))
    return jnp.stack(outs, axis=0)


def solution(mesh):
    in_specs = (P("rcv", "win", None), P(), P("win"))
    out_specs = P("win", None, "rcv")
    return jax.shard_map(shards, mesh=mesh, in_specs=in_specs, out_specs=out_specs, check_vma=False)
```

```python
import math

import jax
import jax.numpy as jnp
from jax import lax
from jax.experimental import pallas as pl
from jax.experimental.pallas import tpu as pltpu
from jax.sharding import PartitionSpec as P

SAMPLES = 6000
HALF = 50
LAGS = 101
ROWS = 128
LANE = 128
FRONT = ROWS - HALF
CHUNK = 2048


def corr_kernel(mq_ref, rt_ref, out_ref, acc_ref, lag_ref, *, scale, pairs, width):
    q = pl.program_id(0)
    u0 = pl.multiple_of(q * width, LANE)
    row = lax.broadcasted_iota(jnp.int32, (ROWS, LANE), 0)
    lane = lax.broadcasted_iota(jnp.int32, (ROWS, LANE), 1)
    keep = lane >= row
    blocks = width // LANE

    def turned(k, b):
        line = mq_ref[pl.ds(k, 1), pl.ds(u0 + b * LANE, LANE)]
        return pltpu.roll(jnp.broadcast_to(line, (ROWS, LANE)), 0, 1, stride=1, stride_axis=0)

    def build(k, slot, half):
        prev = turned(k, 0)
        for b in range(blocks):
            cur = turned(k, b + 1)
            lag_ref[slot, half * ROWS : (half + 1) * ROWS, b * LANE : (b + 1) * LANE] = jnp.where(
                keep, cur, prev
            ).astype(jnp.bfloat16)
            prev = cur

    @pl.when(q == 0)
    def _():
        acc_ref[...] = jnp.zeros_like(acc_ref)

    for p in range(pairs):
        slot = p % 2
        build(2 * p, slot, 0)
        build(2 * p + 1, slot, 1)
        acc_ref[p] += jnp.dot(lag_ref[slot], rt_ref[...], preferred_element_type=jnp.float32)

    @pl.when(q == pl.num_programs(0) - 1)
    def _():
        for k in range(2 * pairs):
            half = (k % 2) * ROWS
            out_ref[k] = acc_ref[k // 2, half : half + LAGS, :] * scale


def correlate(mq, rt, scale):
    n_src = mq.shape[0]
    span, ch = rt.shape
    pairs = n_src // 2
    width = CHUNK if span % CHUNK == 0 else span
    kernel = lambda *refs: corr_kernel(*refs, scale=scale, pairs=pairs, width=width)
    return pl.pallas_call(
        kernel,
        grid=(span // width,),
        in_specs=[
            pl.BlockSpec(mq.shape, lambda q: (0, 0)),
            pl.BlockSpec((width, ch), lambda q: (q, 0)),
        ],
        out_specs=pl.BlockSpec((n_src, LAGS, ch), lambda q: (0, 0, 0)),
        out_shape=jax.ShapeDtypeStruct((n_src, LAGS, ch), jnp.float32),
        scratch_shapes=[
            pltpu.VMEM((pairs, 2 * ROWS, ch), jnp.float32),
            pltpu.VMEM((2, 2 * ROWS, width), jnp.bfloat16),
        ],
        compiler_params=pltpu.CompilerParams(dimension_semantics=("arbitrary",)),
    )(mq, rt)


def gather_sources(picked):
    parts = lax.axis_size("rcv")
    rows, span = picked.shape
    pieces = picked.reshape(rows, parts, span // parts).transpose(1, 0, 2)
    own = lax.all_to_all(pieces, "rcv", 0, 0).sum(axis=0, dtype=jnp.float32)
    spread = jnp.broadcast_to(own.astype(picked.dtype)[None], (parts,) + own.shape)
    every = lax.all_to_all(spread, "rcv", 0, 0)
    return every.transpose(1, 0, 2).reshape(rows, span)


def exchange(part, count):
    me = lax.axis_index("win")
    total = lax.dynamic_index_in_dim(part, me, 0, keepdims=False)
    for d in range(1, count):
        sent = lax.dynamic_index_in_dim(part, (me + d) % count, 0, keepdims=False)
        total = total + lax.ppermute(sent, "win", [(i, (i + d) % count) for i in range(count)])
    return total


def shards(traces, sources, offsets):
    ch_dev = traces.shape[0]
    span = traces.shape[2]
    win_count = lax.axis_size("win")
    first_row = lax.axis_index("rcv") * ch_dev
    norm_scale = 1.0 / math.sqrt(SAMPLES * traces.shape[1] * win_count)
    record = traces[:, 0, :]
    channel_ids = jnp.arange(ch_dev, dtype=jnp.int32)
    select = (sources.reshape(-1)[:, None] - first_row == channel_ids[None, :]).astype(
        traces.dtype
    )
    picked = jnp.dot(select, record, preferred_element_type=jnp.float32).astype(jnp.bfloat16)
    source_rows = gather_sources(picked)
    start_at = offsets[0]
    positions = jnp.arange(span, dtype=jnp.int32)
    inside = (positions >= start_at + HALF) & (positions < start_at + HALF + SAMPLES)
    masked = jnp.where(inside[None, :], source_rows, jnp.zeros_like(source_rows))
    mq = jnp.pad(masked.astype(jnp.float32), ((0, 0), (FRONT, LANE - FRONT)))
    per_group = mq.shape[0] // win_count
    by_group = mq.reshape(win_count, per_group, mq.shape[1])
    rt = record.T
    outs = []
    for i in range(per_group):
        part = correlate(by_group[:, i, :], rt, norm_scale)
        outs.append(exchange(part, win_count))
    return jnp.stack(outs, axis=0)


def solution(mesh):
    in_specs = (P("rcv", "win", None), P(), P("win"))
    out_specs = P("win", None, "rcv")
    return jax.shard_map(shards, mesh=mesh, in_specs=in_specs, out_specs=out_specs, check_vma=False)
```

```python
import math

import jax
import jax.numpy as jnp
from jax import lax
from jax.experimental import pallas as pl
from jax.experimental.pallas import tpu as pltpu
from jax.sharding import PartitionSpec as P

SAMPLES = 6000
HALF = 50
LAGS = 101
ROWS = 128
LANE = 128
FRONT = ROWS - HALF
CHUNK = 2048


def corr_kernel(mq_ref, rt_ref, out_ref, acc_ref, lag_ref, *, scale, pairs, width):
    q = pl.program_id(0)
    u0 = pl.multiple_of(q * width, LANE)
    row = lax.broadcasted_iota(jnp.int32, (ROWS, LANE), 0)
    lane = lax.broadcasted_iota(jnp.int32, (ROWS, LANE), 1)
    keep = lane >= row
    blocks = width // LANE

    def turned(k, b):
        line = mq_ref[pl.ds(k, 1), pl.ds(u0 + b * LANE, LANE)]
        return pltpu.roll(jnp.broadcast_to(line, (ROWS, LANE)), 0, 1, stride=1, stride_axis=0)

    def build(k, slot, half):
        prev = turned(k, 0)
        for b in range(blocks):
            cur = turned(k, b + 1)
            lag_ref[slot, half * ROWS : (half + 1) * ROWS, b * LANE : (b + 1) * LANE] = jnp.where(
                keep, cur, prev
            ).astype(jnp.bfloat16)
            prev = cur

    @pl.when(q == 0)
    def _():
        acc_ref[...] = jnp.zeros_like(acc_ref)

    for p in range(pairs):
        slot = p % 2
        build(2 * p, slot, 0)
        build(2 * p + 1, slot, 1)
        acc_ref[p] += jnp.dot(lag_ref[slot], rt_ref[...], preferred_element_type=jnp.float32)

    @pl.when(q == pl.num_programs(0) - 1)
    def _():
        for k in range(2 * pairs):
            half = (k % 2) * ROWS
            out_ref[k] = acc_ref[k // 2, half : half + LAGS, :] * scale


def correlate(mq, rt, scale):
    n_src = mq.shape[0]
    span, ch = rt.shape
    pairs = n_src // 2
    width = CHUNK if span % CHUNK == 0 else span
    kernel = lambda *refs: corr_kernel(*refs, scale=scale, pairs=pairs, width=width)
    return pl.pallas_call(
        kernel,
        grid=(span // width,),
        in_specs=[
            pl.BlockSpec(mq.shape, lambda q: (0, 0)),
            pl.BlockSpec((width, ch), lambda q: (q, 0)),
        ],
        out_specs=pl.BlockSpec((n_src, LAGS, ch), lambda q: (0, 0, 0)),
        out_shape=jax.ShapeDtypeStruct((n_src, LAGS, ch), jnp.float32),
        scratch_shapes=[
            pltpu.VMEM((pairs, 2 * ROWS, ch), jnp.float32),
            pltpu.VMEM((2, 2 * ROWS, width), jnp.bfloat16),
        ],
        compiler_params=pltpu.CompilerParams(dimension_semantics=("arbitrary",)),
    )(mq, rt)


def gather_sources(picked):
    parts = lax.axis_size("rcv")
    rows, span = picked.shape
    pieces = picked.reshape(rows, parts, span // parts).transpose(1, 0, 2)
    own = lax.all_to_all(pieces, "rcv", 0, 0).sum(axis=0, dtype=jnp.float32)
    spread = jnp.broadcast_to(own.astype(picked.dtype)[None], (parts,) + own.shape)
    every = lax.all_to_all(spread, "rcv", 0, 0)
    return every.transpose(1, 0, 2).reshape(rows, span)


def shards(traces, sources, offsets):
    ch_dev = traces.shape[0]
    span = traces.shape[2]
    win_count = lax.axis_size("win")
    first_row = lax.axis_index("rcv") * ch_dev
    norm_scale = 1.0 / math.sqrt(SAMPLES * traces.shape[1] * win_count)
    record = traces[:, 0, :]
    local = sources.reshape(-1) - first_row
    owned = (local >= 0) & (local < ch_dev)
    rows = jnp.take(record, jnp.clip(local, 0, ch_dev - 1), axis=0)
    picked = jnp.where(owned[:, None], rows, jnp.zeros_like(rows))
    source_rows = gather_sources(picked)
    start_at = offsets[0]
    positions = jnp.arange(span, dtype=jnp.int32)
    inside = (positions >= start_at + HALF) & (positions < start_at + HALF + SAMPLES)
    masked = jnp.where(inside[None, :], source_rows, jnp.zeros_like(source_rows))
    mq = jnp.pad(masked.astype(jnp.float32), ((0, 0), (FRONT, LANE - FRONT)))
    per_group = mq.shape[0] // win_count
    by_group = mq.reshape(win_count, per_group, mq.shape[1])
    rt = record.T
    bounds = [0, 1, 2, per_group] if per_group == 4 else list(range(per_group + 1))
    outs = []
    for lo, hi in zip(bounds[:-1], bounds[1:]):
        chunk = by_group[:, lo:hi, :].reshape(win_count * (hi - lo), mq.shape[1])
        part = correlate(chunk, rt, norm_scale)
        part = part.reshape((win_count, hi - lo) + part.shape[1:])
        outs.append(lax.all_to_all(part, "win", 0, 0).sum(axis=0))
    return jnp.concatenate(outs, axis=0)


def solution(mesh):
    in_specs = (P("rcv", "win", None), P(), P("win"))
    out_specs = P("win", None, "rcv")
    return jax.shard_map(shards, mesh=mesh, in_specs=in_specs, out_specs=out_specs, check_vma=False)
```

```python
import math

import jax
import jax.numpy as jnp
from jax import lax
from jax.experimental import pallas as pl
from jax.experimental.pallas import tpu as pltpu
from jax.sharding import PartitionSpec as P

SAMPLES = 6000
HALF = 50
LAGS = 101
ROWS = 128
LANE = 128
FRONT = ROWS - HALF
CHUNK = 2048
KEPT = 104
PARTS = 2


def corr_kernel(mq_ref, rt_ref, out_ref, acc_ref, lag_ref, *, scale, pairs, width):
    q = pl.program_id(0)
    u0 = pl.multiple_of(q * width, LANE)
    row = lax.broadcasted_iota(jnp.int32, (ROWS, LANE), 0)
    lane = lax.broadcasted_iota(jnp.int32, (ROWS, LANE), 1)
    keep = lane >= row
    blocks = width // LANE

    def turned(k, b):
        line = mq_ref[pl.ds(k, 1), pl.ds(u0 + b * LANE, LANE)]
        return pltpu.roll(jnp.broadcast_to(line, (ROWS, LANE)), 0, 1, stride=1, stride_axis=0)

    def build(k, slot, half):
        prev = turned(k, 0)
        for b in range(blocks):
            cur = turned(k, b + 1)
            lag_ref[slot, half * ROWS : (half + 1) * ROWS, b * LANE : (b + 1) * LANE] = jnp.where(
                keep, cur, prev
            ).astype(jnp.bfloat16)
            prev = cur

    @pl.when(q == 0)
    def _():
        acc_ref[...] = jnp.zeros_like(acc_ref)

    for p in range(pairs):
        slot = p % 2
        build(2 * p, slot, 0)
        build(2 * p + 1, slot, 1)
        acc_ref[p] += jnp.dot(lag_ref[slot], rt_ref[...], preferred_element_type=jnp.float32)

    @pl.when(q == pl.num_programs(0) - 1)
    def _():
        per = 2 * pairs // out_ref.shape[0]
        for k in range(2 * pairs):
            half = (k % 2) * ROWS
            at = (k % per) * KEPT
            out_ref[k // per, at : at + KEPT, :] = acc_ref[k // 2, half : half + KEPT, :] * scale


def correlate(mq, rt, scale, groups):
    n_src = mq.shape[0]
    span, ch = rt.shape
    pairs = n_src // 2
    width = CHUNK if span % CHUNK == 0 else span
    kernel = lambda *refs: corr_kernel(*refs, scale=scale, pairs=pairs, width=width)
    return pl.pallas_call(
        kernel,
        grid=(span // width,),
        in_specs=[
            pl.BlockSpec(mq.shape, lambda q: (0, 0)),
            pl.BlockSpec((width, ch), lambda q: (q, 0)),
        ],
        out_specs=pl.BlockSpec((groups, n_src // groups * KEPT, ch), lambda q: (0, 0, 0)),
        out_shape=jax.ShapeDtypeStruct((groups, n_src // groups * KEPT, ch), jnp.float32),
        scratch_shapes=[
            pltpu.VMEM((pairs, 2 * ROWS, ch), jnp.float32),
            pltpu.VMEM((2, 2 * ROWS, width), jnp.bfloat16),
        ],
        compiler_params=pltpu.CompilerParams(dimension_semantics=("arbitrary",)),
    )(mq, rt)


def gather_sources(picked):
    parts = lax.axis_size("rcv")
    rows, span = picked.shape
    pieces = picked.reshape(rows, parts, span // parts).transpose(1, 0, 2)
    own = lax.all_to_all(pieces, "rcv", 0, 0).sum(axis=0, dtype=jnp.float32)
    spread = jnp.broadcast_to(own.astype(picked.dtype)[None], (parts,) + own.shape)
    every = lax.all_to_all(spread, "rcv", 0, 0)
    return every.transpose(1, 0, 2).reshape(rows, span)


def shards(traces, sources, offsets):
    ch_dev = traces.shape[0]
    span = traces.shape[2]
    win_count = lax.axis_size("win")
    first_row = lax.axis_index("rcv") * ch_dev
    norm_scale = 1.0 / math.sqrt(SAMPLES * traces.shape[1] * win_count)
    record = traces[:, 0, :]
    channel_ids = jnp.arange(ch_dev, dtype=jnp.int32)
    select = (sources.reshape(-1)[:, None] - first_row == channel_ids[None, :]).astype(
        traces.dtype
    )
    picked = jnp.dot(select, record, preferred_element_type=jnp.float32).astype(jnp.bfloat16)
    source_rows = gather_sources(picked)
    start_at = offsets[0]
    positions = jnp.arange(span, dtype=jnp.int32)
    inside = (positions >= start_at + HALF) & (positions < start_at + HALF + SAMPLES)
    masked = jnp.where(inside[None, :], source_rows, jnp.zeros_like(source_rows))
    mq = jnp.pad(masked.astype(jnp.float32), ((0, 0), (FRONT, LANE - FRONT)))
    per_group = mq.shape[0] // win_count
    by_group = mq.reshape(win_count, per_group, mq.shape[1])
    rt = record.T
    parts = PARTS if per_group % PARTS == 0 else per_group
    per = per_group // parts
    outs = []
    for i in range(parts):
        chunk = by_group[:, i * per : (i + 1) * per, :].reshape(win_count * per, mq.shape[1])
        part = correlate(chunk, rt, norm_scale, win_count)
        summed = lax.all_to_all(part, "win", 0, 0).sum(axis=0)
        outs.append(summed.reshape(per, KEPT, summed.shape[-1])[:, :LAGS, :])
    return jnp.concatenate(outs, axis=0)


def solution(mesh):
    in_specs = (P("rcv", "win", None), P(), P("win"))
    out_specs = P("win", None, "rcv")
    return jax.shard_map(shards, mesh=mesh, in_specs=in_specs, out_specs=out_specs, check_vma=False)
```

```python
import math

import jax
import jax.numpy as jnp
from jax import lax
from jax.experimental import pallas as pl
from jax.experimental.pallas import tpu as pltpu
from jax.sharding import PartitionSpec as P

SAMPLES = 6000
HALF = 50
LAGS = 101
ROWS = 128
LANE = 128
FRONT = ROWS - HALF
CHUNK = 2048
KEPT = 104


def corr_kernel(mq_ref, rt_ref, out_ref, acc_ref, lag_ref, *, scale, pairs, width):
    q = pl.program_id(0)
    u0 = pl.multiple_of(q * width, LANE)
    row = lax.broadcasted_iota(jnp.int32, (ROWS, LANE), 0)
    lane = lax.broadcasted_iota(jnp.int32, (ROWS, LANE), 1)
    keep = lane >= row
    blocks = width // LANE

    def turned(k, b):
        line = mq_ref[pl.ds(k, 1), pl.ds(u0 + b * LANE, LANE)]
        return pltpu.roll(jnp.broadcast_to(line, (ROWS, LANE)), 0, 1, stride=1, stride_axis=0)

    def build(k, slot, half):
        prev = turned(k, 0)
        for b in range(blocks):
            cur = turned(k, b + 1)
            lag_ref[slot, half * ROWS : (half + 1) * ROWS, b * LANE : (b + 1) * LANE] = jnp.where(
                keep, cur, prev
            ).astype(jnp.bfloat16)
            prev = cur

    @pl.when(q == 0)
    def _():
        acc_ref[...] = jnp.zeros_like(acc_ref)

    for p in range(pairs):
        slot = p % 2
        build(2 * p, slot, 0)
        build(2 * p + 1, slot, 1)
        acc_ref[p] += jnp.dot(lag_ref[slot], rt_ref[...], preferred_element_type=jnp.float32)

    @pl.when(q == pl.num_programs(0) - 1)
    def _():
        per = 2 * pairs // out_ref.shape[0]
        for k in range(2 * pairs):
            half = (k % 2) * ROWS
            at = (k % per) * KEPT
            out_ref[k // per, at : at + KEPT, :] = acc_ref[k // 2, half : half + KEPT, :] * scale


def correlate(mq, rt, scale, groups):
    n_src = mq.shape[0]
    span, ch = rt.shape
    pairs = n_src // 2
    width = CHUNK if span % CHUNK == 0 else span
    kernel = lambda *refs: corr_kernel(*refs, scale=scale, pairs=pairs, width=width)
    return pl.pallas_call(
        kernel,
        grid=(span // width,),
        in_specs=[
            pl.BlockSpec(mq.shape, lambda q: (0, 0)),
            pl.BlockSpec((width, ch), lambda q: (q, 0)),
        ],
        out_specs=pl.BlockSpec((groups, n_src // groups * KEPT, ch), lambda q: (0, 0, 0)),
        out_shape=jax.ShapeDtypeStruct((groups, n_src // groups * KEPT, ch), jnp.float32),
        scratch_shapes=[
            pltpu.VMEM((pairs, 2 * ROWS, ch), jnp.float32),
            pltpu.VMEM((2, 2 * ROWS, width), jnp.bfloat16),
        ],
        compiler_params=pltpu.CompilerParams(dimension_semantics=("arbitrary",)),
    )(mq, rt)


def gather_sources(picked):
    parts = lax.axis_size("rcv")
    rows, span = picked.shape
    pieces = picked.reshape(rows, parts, span // parts).transpose(1, 0, 2)
    own = lax.all_to_all(pieces, "rcv", 0, 0).sum(axis=0, dtype=jnp.float32)
    spread = jnp.broadcast_to(own.astype(picked.dtype)[None], (parts,) + own.shape)
    every = lax.all_to_all(spread, "rcv", 0, 0)
    return every.transpose(1, 0, 2).reshape(rows, span)


def shards(traces, sources, offsets):
    ch_dev = traces.shape[0]
    span = traces.shape[2]
    win_count = lax.axis_size("win")
    first_row = lax.axis_index("rcv") * ch_dev
    norm_scale = 1.0 / math.sqrt(SAMPLES * traces.shape[1] * win_count)
    record = traces[:, 0, :]
    channel_ids = jnp.arange(ch_dev, dtype=jnp.int32)
    select = (sources.reshape(-1)[:, None] - first_row == channel_ids[None, :]).astype(
        traces.dtype
    )
    picked = jnp.dot(select, record, preferred_element_type=jnp.float32).astype(jnp.bfloat16)
    source_rows = gather_sources(picked)
    start_at = offsets[0]
    positions = jnp.arange(span, dtype=jnp.int32)
    inside = (positions >= start_at + HALF) & (positions < start_at + HALF + SAMPLES)
    masked = jnp.where(inside[None, :], source_rows, jnp.zeros_like(source_rows))
    mq = jnp.pad(masked.astype(jnp.float32), ((0, 0), (FRONT, LANE - FRONT)))
    per_group = mq.shape[0] // win_count
    by_group = mq.reshape(win_count, per_group, mq.shape[1])
    rt = record.T
    bounds = [0, 1, per_group]
    outs = []
    for lo, hi in zip(bounds[:-1], bounds[1:]):
        per = hi - lo
        chunk = by_group[:, lo:hi, :].reshape(win_count * per, mq.shape[1])
        part = correlate(chunk, rt, norm_scale, win_count)
        summed = lax.all_to_all(part, "win", 0, 0).sum(axis=0)
        outs.append(summed.reshape(per, KEPT, summed.shape[-1])[:, :LAGS, :])
    return jnp.concatenate(outs, axis=0)


def solution(mesh):
    in_specs = (P("rcv", "win", None), P(), P("win"))
    out_specs = P("win", None, "rcv")
    return jax.shard_map(shards, mesh=mesh, in_specs=in_specs, out_specs=out_specs, check_vma=False)
```

```python
import math

import jax
import jax.numpy as jnp
from jax import lax
from jax.experimental import pallas as pl
from jax.experimental.pallas import tpu as pltpu
from jax.sharding import PartitionSpec as P

SAMPLES = 6000
HALF = 50
LAGS = 101
ROWS = 128
LANE = 128
FRONT = ROWS - HALF
CHUNK = 2048
STACK = 4
KEPT = 104


def corr_kernel(mq_ref, rt_ref, out_ref, acc_ref, lag_ref, *, scale, sets, width):
    q = pl.program_id(0)
    u0 = pl.multiple_of(q * width, LANE)
    row = lax.broadcasted_iota(jnp.int32, (ROWS, LANE), 0)
    lane = lax.broadcasted_iota(jnp.int32, (ROWS, LANE), 1)
    keep = lane >= row
    blocks = width // LANE

    def turned(k, b):
        line = mq_ref[pl.ds(k, 1), pl.ds(u0 + b * LANE, LANE)]
        return pltpu.roll(jnp.broadcast_to(line, (ROWS, LANE)), 0, 1, stride=1, stride_axis=0)

    def build(k, slot, half):
        prev = turned(k, 0)
        for b in range(blocks):
            cur = turned(k, b + 1)
            lag_ref[slot, half * ROWS : (half + 1) * ROWS, b * LANE : (b + 1) * LANE] = jnp.where(
                keep, cur, prev
            ).astype(jnp.bfloat16)
            prev = cur

    @pl.when(q == 0)
    def _():
        acc_ref[...] = jnp.zeros_like(acc_ref)

    for p in range(sets):
        slot = p % 2
        for i in range(STACK):
            build(STACK * p + i, slot, i)
        acc_ref[p] += jnp.dot(lag_ref[slot], rt_ref[...], preferred_element_type=jnp.float32)

    @pl.when(q == pl.num_programs(0) - 1)
    def _():
        per = STACK * sets // out_ref.shape[0]
        for k in range(STACK * sets):
            top = (k % STACK) * ROWS
            at = (k % per) * KEPT
            out_ref[k // per, at : at + KEPT, :] = acc_ref[k // STACK, top : top + KEPT, :] * scale


def correlate(mq, rt, scale, groups):
    n_src = mq.shape[0]
    span, ch = rt.shape
    sets = n_src // STACK
    width = CHUNK if span % CHUNK == 0 else span
    kernel = lambda *refs: corr_kernel(*refs, scale=scale, sets=sets, width=width)
    return pl.pallas_call(
        kernel,
        grid=(span // width,),
        in_specs=[
            pl.BlockSpec(mq.shape, lambda q: (0, 0)),
            pl.BlockSpec((width, ch), lambda q: (q, 0)),
        ],
        out_specs=pl.BlockSpec((groups, n_src // groups * KEPT, ch), lambda q: (0, 0, 0)),
        out_shape=jax.ShapeDtypeStruct((groups, n_src // groups * KEPT, ch), jnp.float32),
        scratch_shapes=[
            pltpu.VMEM((sets, STACK * ROWS, ch), jnp.float32),
            pltpu.VMEM((2, STACK * ROWS, width), jnp.bfloat16),
        ],
        compiler_params=pltpu.CompilerParams(dimension_semantics=("arbitrary",)),
    )(mq, rt)


def gather_sources(picked):
    parts = lax.axis_size("rcv")
    rows, span = picked.shape
    pieces = picked.reshape(rows, parts, span // parts).transpose(1, 0, 2)
    own = lax.all_to_all(pieces, "rcv", 0, 0).sum(axis=0, dtype=jnp.float32)
    spread = jnp.broadcast_to(own.astype(picked.dtype)[None], (parts,) + own.shape)
    every = lax.all_to_all(spread, "rcv", 0, 0)
    return every.transpose(1, 0, 2).reshape(rows, span)


def shards(traces, sources, offsets):
    ch_dev = traces.shape[0]
    span = traces.shape[2]
    win_count = lax.axis_size("win")
    first_row = lax.axis_index("rcv") * ch_dev
    norm_scale = 1.0 / math.sqrt(SAMPLES * traces.shape[1] * win_count)
    record = traces[:, 0, :]
    channel_ids = jnp.arange(ch_dev, dtype=jnp.int32)
    select = (sources.reshape(-1)[:, None] - first_row == channel_ids[None, :]).astype(
        traces.dtype
    )
    picked = jnp.dot(select, record, preferred_element_type=jnp.float32).astype(jnp.bfloat16)
    source_rows = gather_sources(picked)
    start_at = offsets[0]
    positions = jnp.arange(span, dtype=jnp.int32)
    inside = (positions >= start_at + HALF) & (positions < start_at + HALF + SAMPLES)
    masked = jnp.where(inside[None, :], source_rows, jnp.zeros_like(source_rows))
    mq = jnp.pad(masked.astype(jnp.float32), ((0, 0), (FRONT, LANE - FRONT)))
    per_group = mq.shape[0] // win_count
    by_group = mq.reshape(win_count, per_group, mq.shape[1])
    rt = record.T
    bounds = [0, 1, per_group]
    outs = []
    for lo, hi in zip(bounds[:-1], bounds[1:]):
        per = hi - lo
        chunk = by_group[:, lo:hi, :].reshape(win_count * per, mq.shape[1])
        part = correlate(chunk, rt, norm_scale, win_count)
        summed = lax.all_to_all(part, "win", 0, 0).sum(axis=0)
        outs.append(summed.reshape(per, KEPT, summed.shape[-1])[:, :LAGS, :])
    return jnp.concatenate(outs, axis=0)


def solution(mesh):
    in_specs = (P("rcv", "win", None), P(), P("win"))
    out_specs = P("win", None, "rcv")
    return jax.shard_map(shards, mesh=mesh, in_specs=in_specs, out_specs=out_specs, check_vma=False)
```

```python
import math

import jax
import jax.numpy as jnp
from jax import lax
from jax.experimental import pallas as pl
from jax.experimental.pallas import tpu as pltpu
from jax.sharding import PartitionSpec as P

SAMPLES = 6000
HALF = 50
LAGS = 101
ROWS = 128
LANE = 128
FRONT = ROWS - HALF
CHUNK = 2048


def corr_kernel(mq_ref, rt_ref, out_ref, acc_ref, lag_ref, *, scale, pairs, width, base):
    q = pl.program_id(0)
    u0 = pl.multiple_of(q * width, LANE)
    row = lax.broadcasted_iota(jnp.int32, (ROWS, LANE), 0)
    lane = lax.broadcasted_iota(jnp.int32, (ROWS, LANE), 1)
    keep = lane >= row
    blocks = width // LANE

    def turned(k, b):
        line = mq_ref[pl.ds(base + k, 1), pl.ds(u0 + b * LANE, LANE)].astype(jnp.float32)
        return pltpu.roll(jnp.broadcast_to(line, (ROWS, LANE)), 0, 1, stride=1, stride_axis=0)

    def build(k, slot, half):
        prev = turned(k, 0)
        for b in range(blocks):
            cur = turned(k, b + 1)
            lag_ref[slot, half * ROWS : (half + 1) * ROWS, b * LANE : (b + 1) * LANE] = jnp.where(
                keep, cur, prev
            ).astype(jnp.bfloat16)
            prev = cur

    @pl.when(q == 0)
    def _():
        acc_ref[...] = jnp.zeros_like(acc_ref)

    for p in range(pairs):
        slot = p % 2
        build(2 * p, slot, 0)
        build(2 * p + 1, slot, 1)
        acc_ref[p] += jnp.dot(lag_ref[slot], rt_ref[...], preferred_element_type=jnp.float32)

    @pl.when(q == pl.num_programs(0) - 1)
    def _():
        groups = out_ref.shape[0]
        for k in range(2 * pairs):
            half = (k % 2) * ROWS
            at = (k // groups) * LAGS
            out_ref[k % groups, at : at + LAGS, :] = acc_ref[k // 2, half : half + LAGS, :] * scale


def correlate(mq, rt, scale, groups, base, n_src):
    span, ch = rt.shape
    pairs = n_src // 2
    width = CHUNK if span % CHUNK == 0 else span
    kernel = lambda *refs: corr_kernel(*refs, scale=scale, pairs=pairs, width=width, base=base)
    return pl.pallas_call(
        kernel,
        grid=(span // width,),
        in_specs=[
            pl.BlockSpec(mq.shape, lambda q: (0, 0)),
            pl.BlockSpec((width, ch), lambda q: (q, 0)),
        ],
        out_specs=pl.BlockSpec((groups, n_src // groups * LAGS, ch), lambda q: (0, 0, 0)),
        out_shape=jax.ShapeDtypeStruct((groups, n_src // groups * LAGS, ch), jnp.float32),
        scratch_shapes=[
            pltpu.VMEM((pairs, 2 * ROWS, ch), jnp.float32),
            pltpu.VMEM((2, 2 * ROWS, width), jnp.bfloat16),
        ],
        compiler_params=pltpu.CompilerParams(dimension_semantics=("arbitrary",)),
    )(mq, rt)


def gather_sources(picked):
    parts = lax.axis_size("rcv")
    rows, span = picked.shape
    pieces = picked.reshape(rows, parts, span // parts).transpose(1, 0, 2)
    own = lax.all_to_all(pieces, "rcv", 0, 0).sum(axis=0, dtype=jnp.float32)
    spread = jnp.broadcast_to(own.astype(picked.dtype)[None], (parts,) + own.shape)
    every = lax.all_to_all(spread, "rcv", 0, 0)
    return every.transpose(1, 0, 2).reshape(rows, span)


def shards(traces, sources, offsets):
    ch_dev = traces.shape[0]
    span = traces.shape[2]
    win_count = lax.axis_size("win")
    first_row = lax.axis_index("rcv") * ch_dev
    norm_scale = 1.0 / math.sqrt(SAMPLES * traces.shape[1] * win_count)
    record = traces[:, 0, :]
    channel_ids = jnp.arange(ch_dev, dtype=jnp.int32)
    wanted = sources.T.reshape(-1)
    select = (wanted[:, None] - first_row == channel_ids[None, :]).astype(traces.dtype)
    picked = jnp.dot(select, record, preferred_element_type=jnp.float32).astype(jnp.bfloat16)
    start_at = offsets[0]
    positions = jnp.arange(span, dtype=jnp.int32)
    inside = (positions >= start_at + HALF) & (positions < start_at + HALF + SAMPLES)
    masked = jnp.where(inside[None, :], picked, jnp.zeros_like(picked))
    mq = gather_sources(jnp.pad(masked, ((0, 0), (FRONT, LANE - FRONT))))
    per_group = mq.shape[0] // win_count
    rt = record.T
    bounds = [0, 1, per_group]
    outs = []
    for lo, hi in zip(bounds[:-1], bounds[1:]):
        per = hi - lo
        part = correlate(mq, rt, norm_scale, win_count, lo * win_count, per * win_count)
        summed = lax.all_to_all(part, "win", 0, 0).sum(axis=0)
        outs.append(summed.reshape(per, LAGS, summed.shape[-1]))
    return jnp.concatenate(outs, axis=0)


def solution(mesh):
    in_specs = (P("rcv", "win", None), P(), P("win"))
    out_specs = P("win", None, "rcv")
    return jax.shard_map(shards, mesh=mesh, in_specs=in_specs, out_specs=out_specs, check_vma=False)
```

```python
import math

import jax
import jax.numpy as jnp
from jax import lax
from jax.experimental import pallas as pl
from jax.experimental.pallas import tpu as pltpu
from jax.sharding import PartitionSpec as P

SAMPLES = 6000
HALF = 50
LAGS = 101
ROWS = 128
LANE = 128
FRONT = ROWS - HALF
CHUNK = 2048


def corr_kernel(mq_ref, rt_ref, out_ref, acc_ref, lag_ref, *, scale, pairs, width, base):
    q = pl.program_id(0)
    u0 = pl.multiple_of(q * width, LANE)
    row = lax.broadcasted_iota(jnp.int32, (ROWS, LANE), 0)
    lane = lax.broadcasted_iota(jnp.int32, (ROWS, LANE), 1)
    keep = lane >= row
    blocks = width // LANE

    def turned(k, b):
        line = mq_ref[pl.ds(base + k, 1), pl.ds(u0 + b * LANE, LANE)].astype(jnp.float32)
        return pltpu.roll(jnp.broadcast_to(line, (ROWS, LANE)), 0, 1, stride=1, stride_axis=0)

    def build(k, slot, half):
        prev = turned(k, 0)
        for b in range(blocks):
            cur = turned(k, b + 1)
            lag_ref[slot, half * ROWS : (half + 1) * ROWS, b * LANE : (b + 1) * LANE] = jnp.where(
                keep, cur, prev
            ).astype(jnp.bfloat16)
            prev = cur

    @pl.when(q == 0)
    def _():
        acc_ref[...] = jnp.zeros_like(acc_ref)

    for p in range(pairs):
        slot = p % 2
        build(2 * p, slot, 0)
        build(2 * p + 1, slot, 1)
        acc_ref[p] += jnp.dot(lag_ref[slot], rt_ref[...], preferred_element_type=jnp.float32)

    @pl.when(q == pl.num_programs(0) - 1)
    def _():
        groups = out_ref.shape[0]
        for k in range(2 * pairs):
            half = (k % 2) * ROWS
            at = (k // groups) * LAGS
            out_ref[k % groups, at : at + LAGS, :] = acc_ref[k // 2, half : half + LAGS, :] * scale


def correlate(mq, rt, scale, groups, base, n_src):
    span, ch = rt.shape
    pairs = n_src // 2
    width = CHUNK if span % CHUNK == 0 else span
    kernel = lambda *refs: corr_kernel(*refs, scale=scale, pairs=pairs, width=width, base=base)
    return pl.pallas_call(
        kernel,
        grid=(span // width,),
        in_specs=[
            pl.BlockSpec(mq.shape, lambda q: (0, 0)),
            pl.BlockSpec((width, ch), lambda q: (q, 0)),
        ],
        out_specs=pl.BlockSpec((groups, n_src // groups * LAGS, ch), lambda q: (0, 0, 0)),
        out_shape=jax.ShapeDtypeStruct((groups, n_src // groups * LAGS, ch), jnp.float32),
        scratch_shapes=[
            pltpu.VMEM((pairs, 2 * ROWS, ch), jnp.float32),
            pltpu.VMEM((2, 2 * ROWS, width), jnp.bfloat16),
        ],
        compiler_params=pltpu.CompilerParams(dimension_semantics=("arbitrary",)),
    )(mq, rt)


def gather_sources(picked):
    parts = lax.axis_size("rcv")
    rows, span = picked.shape
    pieces = picked.reshape(rows, parts, span // parts).transpose(1, 0, 2)
    own = lax.all_to_all(pieces, "rcv", 0, 0).sum(axis=0, dtype=jnp.float32)
    spread = jnp.broadcast_to(own.astype(picked.dtype)[None], (parts,) + own.shape)
    every = lax.all_to_all(spread, "rcv", 0, 0)
    return every.transpose(1, 0, 2).reshape(rows, span)


def shards(traces, sources, offsets):
    ch_dev = traces.shape[0]
    span = traces.shape[2]
    win_count = lax.axis_size("win")
    first_row = lax.axis_index("rcv") * ch_dev
    norm_scale = 1.0 / math.sqrt(SAMPLES * traces.shape[1] * win_count)
    record = traces[:, 0, :]
    channel_ids = jnp.arange(ch_dev, dtype=jnp.int32)
    wanted = sources.T.reshape(-1)
    select = (wanted[:, None] - first_row == channel_ids[None, :]).astype(traces.dtype)
    picked = jnp.dot(select, record, preferred_element_type=jnp.float32).astype(jnp.bfloat16)
    start_at = offsets[0]
    positions = jnp.arange(span, dtype=jnp.int32)
    inside = (positions >= start_at + HALF) & (positions < start_at + HALF + SAMPLES)
    source_rows = gather_sources(picked)
    masked = jnp.where(inside[None, :], source_rows, jnp.zeros_like(source_rows))
    mq = jnp.pad(masked, ((0, 0), (FRONT, LANE - FRONT)))
    per_group = mq.shape[0] // win_count
    rt = record.T
    bounds = [0, 1, per_group]
    outs = []
    for lo, hi in zip(bounds[:-1], bounds[1:]):
        per = hi - lo
        part = correlate(mq, rt, norm_scale, win_count, lo * win_count, per * win_count)
        summed = lax.all_to_all(part, "win", 0, 0).sum(axis=0)
        outs.append(summed.reshape(per, LAGS, summed.shape[-1]))
    return jnp.concatenate(outs, axis=0)


def solution(mesh):
    in_specs = (P("rcv", "win", None), P(), P("win"))
    out_specs = P("win", None, "rcv")
    return jax.shard_map(shards, mesh=mesh, in_specs=in_specs, out_specs=out_specs, check_vma=False)
```

```python
import math

import jax
import jax.numpy as jnp
from jax import lax
from jax.experimental import pallas as pl
from jax.experimental.pallas import tpu as pltpu
from jax.sharding import PartitionSpec as P

SAMPLES = 6000
HALF = 50
LAGS = 101
ROWS = 128
LANE = 128
FRONT = ROWS - HALF
CHUNK = 3072


def corr_kernel(mq_ref, rt_ref, out_ref, acc_ref, lag_ref, *, scale, pairs, width, base):
    q = pl.program_id(0)
    u0 = pl.multiple_of(q * width, LANE)
    row = lax.broadcasted_iota(jnp.int32, (ROWS, LANE), 0)
    lane = lax.broadcasted_iota(jnp.int32, (ROWS, LANE), 1)
    keep = lane >= row
    blocks = width // LANE

    def turned(k, b):
        line = mq_ref[pl.ds(base + k, 1), pl.ds(u0 + b * LANE, LANE)].astype(jnp.float32)
        return pltpu.roll(jnp.broadcast_to(line, (ROWS, LANE)), 0, 1, stride=1, stride_axis=0)

    def build(k, slot, half):
        prev = turned(k, 0)
        for b in range(blocks):
            cur = turned(k, b + 1)
            lag_ref[slot, half * ROWS : (half + 1) * ROWS, b * LANE : (b + 1) * LANE] = jnp.where(
                keep, cur, prev
            ).astype(jnp.bfloat16)
            prev = cur

    @pl.when(q == 0)
    def _():
        acc_ref[...] = jnp.zeros_like(acc_ref)

    for p in range(pairs):
        slot = p % 2
        build(2 * p, slot, 0)
        build(2 * p + 1, slot, 1)
        acc_ref[p] += jnp.dot(lag_ref[slot], rt_ref[...], preferred_element_type=jnp.float32)

    @pl.when(q == pl.num_programs(0) - 1)
    def _():
        groups = out_ref.shape[0]
        for k in range(2 * pairs):
            half = (k % 2) * ROWS
            at = (k // groups) * LAGS
            out_ref[k % groups, at : at + LAGS, :] = acc_ref[k // 2, half : half + LAGS, :] * scale


def correlate(mq, rt, scale, groups, base, n_src):
    span, ch = rt.shape
    pairs = n_src // 2
    width = CHUNK if span % CHUNK == 0 else span
    kernel = lambda *refs: corr_kernel(*refs, scale=scale, pairs=pairs, width=width, base=base)
    return pl.pallas_call(
        kernel,
        grid=(span // width,),
        in_specs=[
            pl.BlockSpec(mq.shape, lambda q: (0, 0)),
            pl.BlockSpec((width, ch), lambda q: (q, 0)),
        ],
        out_specs=pl.BlockSpec((groups, n_src // groups * LAGS, ch), lambda q: (0, 0, 0)),
        out_shape=jax.ShapeDtypeStruct((groups, n_src // groups * LAGS, ch), jnp.float32),
        scratch_shapes=[
            pltpu.VMEM((pairs, 2 * ROWS, ch), jnp.float32),
            pltpu.VMEM((2, 2 * ROWS, width), jnp.bfloat16),
        ],
        compiler_params=pltpu.CompilerParams(dimension_semantics=("arbitrary",)),
    )(mq, rt)


def gather_sources(picked):
    parts = lax.axis_size("rcv")
    rows, span = picked.shape
    pieces = picked.reshape(rows, parts, span // parts).transpose(1, 0, 2)
    own = lax.all_to_all(pieces, "rcv", 0, 0).sum(axis=0, dtype=jnp.float32)
    spread = jnp.broadcast_to(own.astype(picked.dtype)[None], (parts,) + own.shape)
    every = lax.all_to_all(spread, "rcv", 0, 0)
    return every.transpose(1, 0, 2).reshape(rows, span)


def shards(traces, sources, offsets):
    ch_dev = traces.shape[0]
    span = traces.shape[2]
    win_count = lax.axis_size("win")
    first_row = lax.axis_index("rcv") * ch_dev
    norm_scale = 1.0 / math.sqrt(SAMPLES * traces.shape[1] * win_count)
    record = traces[:, 0, :]
    channel_ids = jnp.arange(ch_dev, dtype=jnp.int32)
    wanted = sources.T.reshape(-1)
    select = (wanted[:, None] - first_row == channel_ids[None, :]).astype(traces.dtype)
    picked = jnp.dot(select, record, preferred_element_type=jnp.float32).astype(jnp.bfloat16)
    start_at = offsets[0]
    positions = jnp.arange(span, dtype=jnp.int32)
    inside = (positions >= start_at + HALF) & (positions < start_at + HALF + SAMPLES)
    source_rows = gather_sources(picked)
    masked = jnp.where(inside[None, :], source_rows, jnp.zeros_like(source_rows))
    mq = jnp.pad(masked, ((0, 0), (FRONT, LANE - FRONT)))
    per_group = mq.shape[0] // win_count
    rt = record.T
    bounds = [0, 1, per_group]
    outs = []
    for lo, hi in zip(bounds[:-1], bounds[1:]):
        per = hi - lo
        part = correlate(mq, rt, norm_scale, win_count, lo * win_count, per * win_count)
        summed = lax.all_to_all(part, "win", 0, 0).sum(axis=0)
        outs.append(summed.reshape(per, LAGS, summed.shape[-1]))
    return jnp.concatenate(outs, axis=0)


def solution(mesh):
    in_specs = (P("rcv", "win", None), P(), P("win"))
    out_specs = P("win", None, "rcv")
    return jax.shard_map(shards, mesh=mesh, in_specs=in_specs, out_specs=out_specs, check_vma=False)
```

```python
import math

import jax
import jax.numpy as jnp
from jax import lax
from jax.experimental import pallas as pl
from jax.experimental.pallas import tpu as pltpu
from jax.sharding import PartitionSpec as P

SAMPLES = 6000
HALF = 50
LAGS = 101
ROWS = 112
LANE = 128
FRONT = LANE - HALF
CHUNK = 2048


def corr_kernel(mq_ref, rt_ref, out_ref, acc_ref, lag_ref, *, scale, pairs, width, base):
    q = pl.program_id(0)
    u0 = pl.multiple_of(q * width, LANE)
    row = lax.broadcasted_iota(jnp.int32, (ROWS, LANE), 0)
    lane = lax.broadcasted_iota(jnp.int32, (ROWS, LANE), 1)
    keep = lane >= row
    blocks = width // LANE

    def turned(k, b):
        line = mq_ref[pl.ds(base + k, 1), pl.ds(u0 + b * LANE, LANE)].astype(jnp.float32)
        return pltpu.roll(jnp.broadcast_to(line, (ROWS, LANE)), 0, 1, stride=1, stride_axis=0)

    def build(k, slot, half):
        prev = turned(k, 0)
        for b in range(blocks):
            cur = turned(k, b + 1)
            lag_ref[slot, half * ROWS : (half + 1) * ROWS, b * LANE : (b + 1) * LANE] = jnp.where(
                keep, cur, prev
            ).astype(jnp.bfloat16)
            prev = cur

    @pl.when(q == 0)
    def _():
        acc_ref[...] = jnp.zeros_like(acc_ref)

    for p in range(pairs):
        slot = p % 2
        build(2 * p, slot, 0)
        build(2 * p + 1, slot, 1)
        acc_ref[p] += jnp.dot(lag_ref[slot], rt_ref[...], preferred_element_type=jnp.float32)

    @pl.when(q == pl.num_programs(0) - 1)
    def _():
        groups = out_ref.shape[0]
        for k in range(2 * pairs):
            half = (k % 2) * ROWS
            at = (k // groups) * LAGS
            out_ref[k % groups, at : at + LAGS, :] = acc_ref[k // 2, half : half + LAGS, :] * scale


def correlate(mq, rt, scale, groups, base, n_src):
    span, ch = rt.shape
    pairs = n_src // 2
    width = CHUNK if span % CHUNK == 0 else span
    kernel = lambda *refs: corr_kernel(*refs, scale=scale, pairs=pairs, width=width, base=base)
    return pl.pallas_call(
        kernel,
        grid=(span // width,),
        in_specs=[
            pl.BlockSpec(mq.shape, lambda q: (0, 0)),
            pl.BlockSpec((width, ch), lambda q: (q, 0)),
        ],
        out_specs=pl.BlockSpec((groups, n_src // groups * LAGS, ch), lambda q: (0, 0, 0)),
        out_shape=jax.ShapeDtypeStruct((groups, n_src // groups * LAGS, ch), jnp.float32),
        scratch_shapes=[
            pltpu.VMEM((pairs, 2 * ROWS, ch), jnp.float32),
            pltpu.VMEM((2, 2 * ROWS, width), jnp.bfloat16),
        ],
        compiler_params=pltpu.CompilerParams(dimension_semantics=("arbitrary",)),
    )(mq, rt)


def gather_sources(picked):
    parts = lax.axis_size("rcv")
    rows, span = picked.shape
    pieces = picked.reshape(rows, parts, span // parts).transpose(1, 0, 2)
    own = lax.all_to_all(pieces, "rcv", 0, 0).sum(axis=0, dtype=jnp.float32)
    spread = jnp.broadcast_to(own.astype(picked.dtype)[None], (parts,) + own.shape)
    every = lax.all_to_all(spread, "rcv", 0, 0)
    return every.transpose(1, 0, 2).reshape(rows, span)


def shards(traces, sources, offsets):
    ch_dev = traces.shape[0]
    span = traces.shape[2]
    win_count = lax.axis_size("win")
    first_row = lax.axis_index("rcv") * ch_dev
    norm_scale = 1.0 / math.sqrt(SAMPLES * traces.shape[1] * win_count)
    record = traces[:, 0, :]
    channel_ids = jnp.arange(ch_dev, dtype=jnp.int32)
    wanted = sources.T.reshape(-1)
    select = (wanted[:, None] - first_row == channel_ids[None, :]).astype(traces.dtype)
    picked = jnp.dot(select, record, preferred_element_type=jnp.float32).astype(jnp.bfloat16)
    start_at = offsets[0]
    positions = jnp.arange(span, dtype=jnp.int32)
    inside = (positions >= start_at + HALF) & (positions < start_at + HALF + SAMPLES)
    source_rows = gather_sources(picked)
    masked = jnp.where(inside[None, :], source_rows, jnp.zeros_like(source_rows))
    mq = jnp.pad(masked, ((0, 0), (FRONT, LANE - FRONT)))
    per_group = mq.shape[0] // win_count
    rt = record.T
    bounds = [0, 1, per_group]
    outs = []
    for lo, hi in zip(bounds[:-1], bounds[1:]):
        per = hi - lo
        part = correlate(mq, rt, norm_scale, win_count, lo * win_count, per * win_count)
        summed = lax.all_to_all(part, "win", 0, 0).sum(axis=0)
        outs.append(summed.reshape(per, LAGS, summed.shape[-1]))
    return jnp.concatenate(outs, axis=0)


def solution(mesh):
    in_specs = (P("rcv", "win", None), P(), P("win"))
    out_specs = P("win", None, "rcv")
    return jax.shard_map(shards, mesh=mesh, in_specs=in_specs, out_specs=out_specs, check_vma=False)
```

```python
import math

import jax
import jax.numpy as jnp
from jax import lax
from jax.experimental import pallas as pl
from jax.experimental.pallas import tpu as pltpu
from jax.sharding import PartitionSpec as P

SAMPLES = 6000
HALF = 50
LAGS = 101
ROWS = 104
LANE = 128
FRONT = LANE - HALF
CHUNK = 2048


def corr_kernel(mq_ref, rt_ref, out_ref, acc_ref, lag_ref, *, scale, pairs, width, base):
    q = pl.program_id(0)
    u0 = pl.multiple_of(q * width, LANE)
    row = lax.broadcasted_iota(jnp.int32, (ROWS, LANE), 0)
    lane = lax.broadcasted_iota(jnp.int32, (ROWS, LANE), 1)
    keep = lane >= row
    blocks = width // LANE

    def turned(k, b):
        line = mq_ref[pl.ds(base + k, 1), pl.ds(u0 + b * LANE, LANE)].astype(jnp.float32)
        return pltpu.roll(jnp.broadcast_to(line, (ROWS, LANE)), 0, 1, stride=1, stride_axis=0)

    def build(k, slot, half):
        prev = turned(k, 0)
        for b in range(blocks):
            cur = turned(k, b + 1)
            lag_ref[slot, half * ROWS : (half + 1) * ROWS, b * LANE : (b + 1) * LANE] = jnp.where(
                keep, cur, prev
            ).astype(jnp.bfloat16)
            prev = cur

    @pl.when(q == 0)
    def _():
        acc_ref[...] = jnp.zeros_like(acc_ref)

    for p in range(pairs):
        slot = p % 2
        build(2 * p, slot, 0)
        build(2 * p + 1, slot, 1)
        acc_ref[p] += jnp.dot(lag_ref[slot], rt_ref[...], preferred_element_type=jnp.float32)

    @pl.when(q == pl.num_programs(0) - 1)
    def _():
        groups = out_ref.shape[0]
        for k in range(2 * pairs):
            half = (k % 2) * ROWS
            at = (k // groups) * LAGS
            out_ref[k % groups, at : at + LAGS, :] = acc_ref[k // 2, half : half + LAGS, :] * scale


def correlate(mq, rt, scale, groups, base, n_src):
    span, ch = rt.shape
    pairs = n_src // 2
    width = CHUNK if span % CHUNK == 0 else span
    kernel = lambda *refs: corr_kernel(*refs, scale=scale, pairs=pairs, width=width, base=base)
    return pl.pallas_call(
        kernel,
        grid=(span // width,),
        in_specs=[
            pl.BlockSpec(mq.shape, lambda q: (0, 0)),
            pl.BlockSpec((width, ch), lambda q: (q, 0)),
        ],
        out_specs=pl.BlockSpec((groups, n_src // groups * LAGS, ch), lambda q: (0, 0, 0)),
        out_shape=jax.ShapeDtypeStruct((groups, n_src // groups * LAGS, ch), jnp.float32),
        scratch_shapes=[
            pltpu.VMEM((pairs, 2 * ROWS, ch), jnp.float32),
            pltpu.VMEM((2, 2 * ROWS, width), jnp.bfloat16),
        ],
        compiler_params=pltpu.CompilerParams(dimension_semantics=("arbitrary",)),
    )(mq, rt)


def gather_sources(picked):
    parts = lax.axis_size("rcv")
    rows, span = picked.shape
    pieces = picked.reshape(rows, parts, span // parts).transpose(1, 0, 2)
    own = lax.all_to_all(pieces, "rcv", 0, 0).sum(axis=0, dtype=jnp.float32)
    spread = jnp.broadcast_to(own.astype(picked.dtype)[None], (parts,) + own.shape)
    every = lax.all_to_all(spread, "rcv", 0, 0)
    return every.transpose(1, 0, 2).reshape(rows, span)


def shards(traces, sources, offsets):
    ch_dev = traces.shape[0]
    span = traces.shape[2]
    win_count = lax.axis_size("win")
    first_row = lax.axis_index("rcv") * ch_dev
    norm_scale = 1.0 / math.sqrt(SAMPLES * traces.shape[1] * win_count)
    record = traces[:, 0, :]
    channel_ids = jnp.arange(ch_dev, dtype=jnp.int32)
    wanted = sources.T.reshape(-1)
    select = (wanted[:, None] - first_row == channel_ids[None, :]).astype(traces.dtype)
    picked = jnp.dot(select, record, preferred_element_type=jnp.float32).astype(jnp.bfloat16)
    start_at = offsets[0]
    positions = jnp.arange(span, dtype=jnp.int32)
    inside = (positions >= start_at + HALF) & (positions < start_at + HALF + SAMPLES)
    source_rows = gather_sources(picked)
    masked = jnp.where(inside[None, :], source_rows, jnp.zeros_like(source_rows))
    mq = jnp.pad(masked, ((0, 0), (FRONT, LANE - FRONT)))
    per_group = mq.shape[0] // win_count
    rt = record.T
    bounds = [0, 1, per_group]
    outs = []
    for lo, hi in zip(bounds[:-1], bounds[1:]):
        per = hi - lo
        part = correlate(mq, rt, norm_scale, win_count, lo * win_count, per * win_count)
        summed = lax.all_to_all(part, "win", 0, 0).sum(axis=0)
        outs.append(summed.reshape(per, LAGS, summed.shape[-1]))
    return jnp.concatenate(outs, axis=0)


def solution(mesh):
    in_specs = (P("rcv", "win", None), P(), P("win"))
    out_specs = P("win", None, "rcv")
    return jax.shard_map(shards, mesh=mesh, in_specs=in_specs, out_specs=out_specs, check_vma=False)
```
